512 devices in a mesh: ta: 32 (over x_hi, z), gz: 8 (over y, x_lo), gy: 2 (over core).
Axes of the slice: x: 4 (x_hi: 2, x_lo: 2; x = x_hi * 2 + x_lo), y: 4, z: 16, core: 2. Of those that a mesh axis runs over, the one named last changes fastest.
Arguments:
- source_field: bfloat16 [32, 16, 4, 2, 256, 128], P('ta', 'gz', 'gy'), may hold values from -6 to 6
- clover: bfloat16 [32, 16, 4, 2, 128, 128], P('ta', 'gz', 'gy'), may hold values from -0.1875 to 0.1875
- forward: bfloat16 [4, 32, 16, 4, 2, 128, 128], P(None, 'ta', 'gz', 'gy'), may hold values from -0.1875 to 0.1875
- backward: bfloat16 [4, 32, 16, 4, 2, 128, 128], P(None, 'ta', 'gz', 'gy'), may hold values from -0.1875 to 0.1875
- restrict_blocks: bfloat16 [32, 16, 4, 2, 128, 128], P('ta', 'gz', 'gy'), may hold values from -0.1875 to 0.1875
Outputs:
- second_image: bfloat16 [32, 16, 4, 2, 256, 128], P('ta', 'gz', 'gy')
- restricted: bfloat16 [32, 16, 256, 128], P('ta')
The draws below stay inside these ranges and needn't reach their ends.
All inputs are finite; a program needn't handle non-finite values.
Results may differ from the reference program's by a relative error of at most 0.0064.
Values may be sent and summed in bfloat16 or wider, within the bound.
No kernel may reach another device: no remote copies, remote signals or barrier semaphores. Data moves between devices by JAX's collectives and lax.ppermute only.
A program may use at most 64 MiB of HBM per device.

```python
import jax
import jax.numpy as jnp
from jax import lax

NV = 128
NR = 256
LT = 1
LZ = 2
LY = 2
LX = 2
NT = 32
NZ = 16
NY = 4
N_TA = 32
N_GZ = 8
N_GY = 2


def block_levels(stream_key, dims, cuts, least, high):
    loudness, own = 1.0, jax.random.fold_in(stream_key, 6)
    for position, parts in cuts:
        heights = jnp.exp(jax.random.uniform(jax.random.fold_in(own, position), (parts,), jnp.float32, least / len(cuts), high / len(cuts)))
        loudness = loudness * jnp.repeat(heights, dims[position] // parts).reshape([-1 if axis == position else 1 for axis in range(len(dims))])
    return loudness


def noise(stream_key, shape, width, bound, split=(), kind=jnp.bfloat16):
    result = width * jax.random.normal(stream_key, shape, jnp.float32)
    if split:
        result = result * block_levels(stream_key, shape, split, -0.22, 0.18)
    return jnp.clip(result, -bound, bound).astype(kind)


def setup_inputs(seed: int = 0) -> dict:
    key_of = jax.random.split(jax.random.key(seed), 6)
    return {
        "source_field": noise(key_of[0], (NT, NZ, NY, LX, NR, NV), 1.0, 6.0, ((0, 32), (1, 8), (2, 2))),
        "clover": noise(key_of[1], (NT, NZ, NY, LX, NV, NV), (9 * NV) ** -0.5, 0.1875, ((0, 32), (1, 8), (2, 2))),
        "forward": noise(key_of[2], (4, NT, NZ, NY, LX, NV, NV), (9 * NV) ** -0.5, 0.1875, ((1, 32), (2, 8), (3, 2))),
        "backward": noise(key_of[3], (4, NT, NZ, NY, LX, NV, NV), (9 * NV) ** -0.5, 0.1875, ((1, 32), (2, 8), (3, 2))),
        "restrict_blocks": noise(key_of[4], (NT, NZ, NY, LX, NV, NV), (LT * LZ * LY * LX * NV) ** -0.5, 0.1875, ((0, 32), (1, 8), (2, 2))),
    }


def apply_block(blocks, vector):
    return jnp.einsum('tzyxij,tzyxrj->tzyxri', blocks.astype(jnp.float32), vector.astype(jnp.float32))


def operate(vector, clover, forward, backward):
    total = apply_block(clover, vector)
    for axis_id in range(4):
        total = total + apply_block(forward[axis_id], jnp.roll(vector, -1, axis=axis_id))
        formed = lax.optimization_barrier(apply_block(backward[axis_id], vector).astype(jnp.bfloat16))
        total = total + jnp.roll(formed.astype(jnp.float32), 1, axis=axis_id)
    return total.astype(jnp.bfloat16)


def reference(source_field, clover, forward, backward, restrict_blocks):
    first_image = operate(source_field, clover, forward, backward)
    second_image = operate(first_image, clover, forward, backward)
    blocks = restrict_blocks.astype(jnp.float32).reshape(N_TA, LT, N_GZ, LZ, N_GY, LY, LX, NV, NV)
    values = second_image.astype(jnp.float32).reshape(N_TA, LT, N_GZ, LZ, N_GY, LY, LX, NR, NV)
    summed = jnp.einsum('apbqcrxij,apbqcrxkj->abcki', blocks, values)
    restricted = summed.reshape(N_TA, N_GZ * N_GY, NR, NV).astype(jnp.bfloat16)
    return second_image, restricted
```

```python
import jax
import jax.numpy as jnp
from jax import lax
from jax.sharding import PartitionSpec as P


def apply_block(blocks, vector):
    return jnp.einsum("tzyxij,tzyxrj->tzyxri", blocks, vector, preferred_element_type=jnp.float32)


def formed(blocks, vector):
    return lax.optimization_barrier(apply_block(blocks, vector).astype(jnp.bfloat16))


def ring(n, step):
    return [(i, (i + step) % n) for i in range(n)]


def take(block, dim, start, stop):
    return lax.slice_in_dim(block, start, stop, axis=dim)


def neighbours(vector, pulled, dim, axis):
    count = lax.axis_size(axis)
    size = vector.shape[dim]
    first = take(vector, dim, 0, 1)
    last = take(pulled, dim, size - 1, size)
    if count == 2:
        both = lax.ppermute(jnp.stack([first, last]), axis, ring(2, 1))
        got_v, got_p = both[0], both[1]
    else:
        got_v = lax.ppermute(first, axis, ring(count, -1))
        got_p = lax.ppermute(last, axis, ring(count, 1))
    ahead = jnp.concatenate([take(vector, dim, 1, size), got_v], axis=dim)
    behind = jnp.concatenate([got_p, take(pulled, dim, 0, size - 1)], axis=dim)
    return ahead, behind


def operate(vector, clover, forward, backward):
    pulled = [formed(backward[m], vector) for m in range(4)]
    terms = []
    pulls = []
    for m, axis in ((0, "ta"), (1, "gz"), (2, "gy")):
        ahead, behind = neighbours(vector, pulled[m], m, axis)
        terms.append(apply_block(forward[m], ahead))
        pulls.append(behind)
    terms.append(apply_block(forward[3], jnp.roll(vector, -1, axis=3)))
    pulls.append(jnp.roll(pulled[3], 1, axis=3))
    total = apply_block(clover, vector)
    for term in terms:
        total = total + term
    for pull in pulls:
        total = total + pull.astype(jnp.float32)
    return total.astype(jnp.bfloat16)


def gather_pieces(piece):
    nz = lax.axis_size("gz")
    ny = lax.axis_size("gy")
    assert nz == 8 and ny == 2
    g = lax.axis_index("gz")
    c = lax.axis_index("gy")
    other = lax.ppermute(piece, "gz", [(i, i ^ 1) for i in range(nz)])
    pair = jnp.where(g % 2 == 1, jnp.stack([other, piece]), jnp.stack([piece, other]))
    from_prev = lax.ppermute(pair, "gz", ring(nz, 2))
    from_next = lax.ppermute(pair, "gz", ring(nz, -2))
    from_far = lax.ppermute(from_prev, "gz", ring(nz, 2))
    rel = jnp.stack([pair, from_next, from_far, from_prev])
    pairs = nz // 2
    doubled = jnp.concatenate([rel, rel], axis=0)
    absolute = lax.dynamic_slice_in_dim(doubled, pairs - g // 2, pairs, axis=0)
    absolute = absolute.reshape(nz, *piece.shape)
    partner = lax.ppermute(absolute, "gy", ring(2, 1))
    full = jnp.where(
        c == 0, jnp.stack([absolute, partner], axis=1), jnp.stack([partner, absolute], axis=1)
    )
    return full.reshape(1, nz * ny, *piece.shape)


def per_device(source_field, clover, forward, backward, restrict_blocks):
    first_image = operate(source_field, clover, forward, backward)
    second_image = operate(first_image, clover, forward, backward)
    partial_sum = jnp.einsum(
        "tzyxij,tzyxrj->ri", restrict_blocks, second_image, preferred_element_type=jnp.float32
    )
    restricted = gather_pieces(partial_sum.astype(jnp.bfloat16))
    return (second_image, restricted)


def solution(mesh):
    return jax.shard_map(
        per_device,
        mesh=mesh,
        in_specs=(
            P("ta", "gz", "gy", None, None, None),
            P("ta", "gz", "gy", None, None, None),
            P(None, "ta", "gz", "gy", None, None, None),
            P(None, "ta", "gz", "gy", None, None, None),
            P("ta", "gz", "gy", None, None, None),
        ),
        out_specs=(P("ta", "gz", "gy", None, None, None), P("ta", None, None, None)),
        check_vma=False,
    )
```

```python
import jax
import jax.numpy as jnp
from jax import lax
from jax.sharding import PartitionSpec as P


def apply_block(blocks, vector):
    return jnp.einsum("tzyxij,tzyxrj->tzyxri", blocks, vector, preferred_element_type=jnp.float32)


def formed(blocks, vector):
    return lax.optimization_barrier(apply_block(blocks, vector).astype(jnp.bfloat16))


def ring(n, step):
    return [(i, (i + step) % n) for i in range(n)]


def take(block, dim, start, stop):
    return lax.slice_in_dim(block, start, stop, axis=dim)


def neighbours(vector, pulled, dim, axis):
    count = lax.axis_size(axis)
    size = vector.shape[dim]
    first = take(vector, dim, 0, 1)
    last = take(pulled, dim, size - 1, size)
    if count == 2:
        both = lax.ppermute(jnp.stack([first, last]), axis, ring(2, 1))
        got_v, got_p = both[0], both[1]
    else:
        got_v = lax.ppermute(first, axis, ring(count, -1))
        got_p = lax.ppermute(last, axis, ring(count, 1))
    ahead = jnp.concatenate([take(vector, dim, 1, size), got_v], axis=dim)
    behind = jnp.concatenate([got_p, take(pulled, dim, 0, size - 1)], axis=dim)
    return ahead, behind


AXES = ((0, "ta"), (1, "gz"), (2, "gy"))


def operate(vector, clover, forward, backward):
    pulled = [formed(backward[m], vector) for m in range(4)]
    terms = []
    pulls = []
    for m, axis in AXES:
        ahead, behind = neighbours(vector, pulled[m], m, axis)
        terms.append(apply_block(forward[m], ahead))
        pulls.append(behind)
    terms.append(apply_block(forward[3], jnp.roll(vector, -1, axis=3)))
    pulls.append(jnp.roll(pulled[3], 1, axis=3))
    total = apply_block(clover, vector)
    for term in terms:
        total = total + term
    for pull in pulls:
        total = total + pull.astype(jnp.float32)
    return total.astype(jnp.bfloat16)


def gather_pieces(piece):
    nz = lax.axis_size("gz")
    ny = lax.axis_size("gy")
    assert nz == 8 and ny == 2
    g = lax.axis_index("gz")
    c = lax.axis_index("gy")
    other = lax.ppermute(piece, "gz", [(i, i ^ 1) for i in range(nz)])
    pair = jnp.where(g % 2 == 1, jnp.stack([other, piece]), jnp.stack([piece, other]))
    from_far = lax.ppermute(pair, "gz", ring(nz, 4))
    from_prev = lax.ppermute(pair, "gz", ring(nz, 2))
    from_next = lax.ppermute(pair, "gz", ring(nz, -2))
    rel = jnp.stack([pair, from_next, from_far, from_prev])
    pairs = nz // 2
    doubled = jnp.concatenate([rel, rel], axis=0)
    absolute = lax.dynamic_slice_in_dim(doubled, pairs - g // 2, pairs, axis=0)
    absolute = absolute.reshape(nz, *piece.shape)
    partner = lax.ppermute(absolute, "gy", ring(2, 1))
    full = jnp.where(
        c == 0, jnp.stack([absolute, partner], axis=1), jnp.stack([partner, absolute], axis=1)
    )
    return full.reshape(1, nz * ny, *piece.shape)


def per_device_body(source_field, clover, forward, backward, restrict_blocks):
    first_image = operate(source_field, clover, forward, backward)
    second_image = operate(first_image, clover, forward, backward)
    partial_sum = jnp.einsum(
        "tzyxij,tzyxrj->ri", restrict_blocks, second_image, preferred_element_type=jnp.float32
    )
    restricted = gather_pieces(partial_sum.astype(jnp.bfloat16))
    return (second_image, restricted)


def solution(mesh):
    return jax.shard_map(
        per_device_body,
        mesh=mesh,
        in_specs=(
            P("ta", "gz", "gy", None, None, None),
            P("ta", "gz", "gy", None, None, None),
            P(None, "ta", "gz", "gy", None, None, None),
            P(None, "ta", "gz", "gy", None, None, None),
            P("ta", "gz", "gy", None, None, None),
        ),
        out_specs=(P("ta", "gz", "gy", None, None, None), P("ta", None, None, None)),
        check_vma=False,
    )
```

```python
import jax
import jax.numpy as jnp
from jax import lax
from jax.sharding import PartitionSpec as P


def apply_block(blocks, vector):
    return jnp.einsum("tzyxij,tzyxrj->tzyxri", blocks, vector, preferred_element_type=jnp.float32)


def formed(blocks, vector):
    return lax.optimization_barrier(apply_block(blocks, vector).astype(jnp.bfloat16))


def ring(n, step):
    return [(i, (i + step) % n) for i in range(n)]


def take(block, dim, start, stop):
    return lax.slice_in_dim(block, start, stop, axis=dim)


def neighbours(vector, pulled, dim, axis):
    count = lax.axis_size(axis)
    size = vector.shape[dim]
    first = take(vector, dim, 0, 1)
    last = take(pulled, dim, size - 1, size)
    if count == 2:
        both = lax.ppermute(jnp.stack([first, last]), axis, ring(2, 1))
        got_v, got_p = both[0], both[1]
    else:
        got_v = lax.ppermute(first, axis, ring(count, -1))
        got_p = lax.ppermute(last, axis, ring(count, 1))
    ahead = jnp.concatenate([take(vector, dim, 1, size), got_v], axis=dim)
    behind = jnp.concatenate([got_p, take(pulled, dim, 0, size - 1)], axis=dim)
    return ahead, behind


AXES = ((0, "ta"), (1, "gz"), (2, "gy"))


def operate(vector, clover, forward, backward):
    pulled = [formed(backward[m], vector) for m in range(4)]
    terms = []
    pulls = []
    for m, axis in AXES:
        ahead, behind = neighbours(vector, pulled[m], m, axis)
        terms.append(apply_block(forward[m], ahead))
        pulls.append(behind)
    terms.append(apply_block(forward[3], jnp.roll(vector, -1, axis=3)))
    pulls.append(jnp.roll(pulled[3], 1, axis=3))
    total = apply_block(clover, vector)
    for term in terms:
        total = total + term
    for pull in pulls:
        total = total + pull.astype(jnp.float32)
    return total.astype(jnp.bfloat16)


def gather_pieces(piece):
    count = lax.axis_size("gz") * lax.axis_size("gy")
    copies = jnp.broadcast_to(piece[None], (count, *piece.shape))
    gathered = lax.all_to_all(copies, ("gz", "gy"), 0, 0, tiled=True)
    return gathered.reshape(1, count, *piece.shape)


def per_device_body(source_field, clover, forward, backward, restrict_blocks):
    first_image = operate(source_field, clover, forward, backward)
    second_image = operate(first_image, clover, forward, backward)
    partial_sum = jnp.einsum(
        "tzyxij,tzyxrj->ri", restrict_blocks, second_image, preferred_element_type=jnp.float32
    )
    restricted = gather_pieces(partial_sum.astype(jnp.bfloat16))
    return (second_image, restricted)


def solution(mesh):
    return jax.shard_map(
        per_device_body,
        mesh=mesh,
        in_specs=(
            P("ta", "gz", "gy", None, None, None),
            P("ta", "gz", "gy", None, None, None),
            P(None, "ta", "gz", "gy", None, None, None),
            P(None, "ta", "gz", "gy", None, None, None),
            P("ta", "gz", "gy", None, None, None),
        ),
        out_specs=(P("ta", "gz", "gy", None, None, None), P("ta", None, None, None)),
        check_vma=False,
    )
```

```python
import jax
import jax.numpy as jnp
from jax import lax
from jax.sharding import PartitionSpec as P


def apply_block(blocks, vector):
    return jnp.einsum("tzyxij,tzyxrj->tzyxri", blocks, vector, preferred_element_type=jnp.float32)


def formed(blocks, vector):
    return lax.optimization_barrier(apply_block(blocks, vector).astype(jnp.bfloat16))


def ring(n, step):
    return [(i, (i + step) % n) for i in range(n)]


def take(block, dim, start, stop):
    return lax.slice_in_dim(block, start, stop, axis=dim)


def send(block, axis, perm):
    return lax.ppermute(block, axis, perm)


def neighbours(vector, pulled, dim, axis):
    count = lax.axis_size(axis)
    size = vector.shape[dim]
    first = take(vector, dim, 0, 1)
    last = take(pulled, dim, size - 1, size)
    if count == 2:
        both = send(jnp.stack([first, last]), axis, ring(2, 1))
        got_v, got_p = both[0], both[1]
    else:
        got_v = send(first, axis, ring(count, -1))
        got_p = send(last, axis, ring(count, 1))
    ahead = jnp.concatenate([take(vector, dim, 1, size), got_v], axis=dim)
    behind = jnp.concatenate([got_p, take(pulled, dim, 0, size - 1)], axis=dim)
    return ahead, behind


AXES = ((0, "ta"), (1, "gz"), (2, "gy"))
ALL = ("ta", "gz", "gy")


def relay_routes(nt, nz, ny):
    half = nt // 2

    def lin(t, g, c):
        return (t * nz + g) * ny + c

    first, second = [], []
    for y in range(nz // 2):
        for c in range(ny):
            for src, mid, dst in (
                ((nt - 1, 0), (half - 1, 1), (0, 0)),
                ((nt - 1, 1), (nt - 1, 0), (0, 1)),
                ((half, 0), (0, 1), (half - 1, 0)),
                ((half, 1), (half, 0), (half - 1, 1)),
            ):
                a, b, d = (lin(t, 2 * y + x, c) for t, x in (src, mid, dst))
                first.append((a, b))
                second.append((b, d))
    return first, second


def time_neighbours(vector, pulled):
    nt, nz, ny = (lax.axis_size(a) for a in ALL)
    size = vector.shape[0]
    first = take(vector, 0, 0, 1)
    last = take(pulled, 0, size - 1, size)
    half = nt // 2
    t = lax.axis_index("ta")
    got_v = send(first, "ta", [(i, (i - 1) % nt) for i in range(nt) if i != half])
    got_p = send(last, "ta", [(i, (i + 1) % nt) for i in range(nt) if i != nt - 1])
    hop_1, hop_2 = relay_routes(nt, nz, ny)
    moving = jnp.where(t == nt - 1, last, first)
    moved = send(send(moving, ALL, hop_1), ALL, hop_2)
    got_p = jnp.where(t == 0, moved, got_p)
    got_v = jnp.where(t == half - 1, moved, got_v)
    ahead = jnp.concatenate([take(vector, 0, 1, size), got_v], axis=0)
    behind = jnp.concatenate([got_p, take(pulled, 0, 0, size - 1)], axis=0)
    return ahead, behind


def operate(vector, clover, forward, backward):
    pulled = [formed(backward[m], vector) for m in range(4)]
    terms = []
    pulls = []
    for m, axis in AXES:
        if axis == "ta":
            ahead, behind = time_neighbours(vector, pulled[m])
        else:
            ahead, behind = neighbours(vector, pulled[m], m, axis)
        terms.append(apply_block(forward[m], ahead))
        pulls.append(behind)
    terms.append(apply_block(forward[3], jnp.roll(vector, -1, axis=3)))
    pulls.append(jnp.roll(pulled[3], 1, axis=3))
    total = apply_block(clover, vector)
    for term in terms:
        total = total + term
    for pull in pulls:
        total = total + pull.astype(jnp.float32)
    return total.astype(jnp.bfloat16)


def gather_pieces(piece):
    count = lax.axis_size("gz") * lax.axis_size("gy")
    copies = jnp.broadcast_to(piece[None], (count, *piece.shape))
    gathered = lax.all_to_all(copies, ("gz", "gy"), 0, 0, tiled=True)
    return gathered.reshape(1, count, *piece.shape)


def per_device_body(source_field, clover, forward, backward, restrict_blocks):
    first_image = operate(source_field, clover, forward, backward)
    second_image = operate(first_image, clover, forward, backward)
    partial_sum = jnp.einsum(
        "tzyxij,tzyxrj->ri", restrict_blocks, second_image, preferred_element_type=jnp.float32
    )
    restricted = gather_pieces(partial_sum.astype(jnp.bfloat16))
    return (second_image, restricted)


def solution(mesh):
    return jax.shard_map(
        per_device_body,
        mesh=mesh,
        in_specs=(
            P("ta", "gz", "gy", None, None, None),
            P("ta", "gz", "gy", None, None, None),
            P(None, "ta", "gz", "gy", None, None, None),
            P(None, "ta", "gz", "gy", None, None, None),
            P("ta", "gz", "gy", None, None, None),
        ),
        out_specs=(P("ta", "gz", "gy", None, None, None), P("ta", None, None, None)),
        check_vma=False,
    )
```

```python
import jax
import jax.numpy as jnp
from jax import lax
from jax.sharding import PartitionSpec as P


def apply_block(blocks, vector):
    return jnp.einsum("tzyxij,tzyxrj->tzyxri", blocks, vector, preferred_element_type=jnp.float32)


def formed(blocks, vector):
    return lax.optimization_barrier(apply_block(blocks, vector).astype(jnp.bfloat16))


def ring(n, step):
    return [(i, (i + step) % n) for i in range(n)]


def take(block, dim, start, stop):
    return lax.slice_in_dim(block, start, stop, axis=dim)


def neighbours(vector, pulled, dim, axis):
    count = lax.axis_size(axis)
    size = vector.shape[dim]
    first = take(vector, dim, 0, 1)
    last = take(pulled, dim, size - 1, size)
    if count == 2:
        both = lax.ppermute(jnp.stack([first, last]), axis, ring(2, 1))
        got_v, got_p = both[0], both[1]
    else:
        got_v = lax.ppermute(first, axis, ring(count, -1))
        got_p = lax.ppermute(last, axis, ring(count, 1))
    ahead = jnp.concatenate([take(vector, dim, 1, size), got_v], axis=dim)
    behind = jnp.concatenate([got_p, take(pulled, dim, 0, size - 1)], axis=dim)
    return ahead, behind


AXES = ((0, "ta"), (1, "gz"), (2, "gy"))


def operate(vector, clover, forward, backward):
    pulled = [formed(backward[m], vector) for m in range(4)]
    terms = []
    pulls = []
    for m, axis in AXES:
        ahead, behind = neighbours(vector, pulled[m], m, axis)
        terms.append(apply_block(forward[m], ahead))
        pulls.append(behind)
    terms.append(apply_block(forward[3], jnp.roll(vector, -1, axis=3)))
    pulls.append(jnp.roll(pulled[3], 1, axis=3))
    total = apply_block(clover, vector)
    for term in terms:
        total = total + term
    for pull in pulls:
        total = total + pull.astype(jnp.float32)
    return total.astype(jnp.bfloat16)


def gather_pieces(piece):
    nz = lax.axis_size("gz")
    assert lax.axis_size("gy") == 2
    copies = jnp.broadcast_to(piece[None], (nz, *piece.shape))
    column = lax.all_to_all(copies, "gz", 0, 0, tiled=True)
    partner = lax.ppermute(column, "gy", ring(2, 1))
    first = lax.axis_index("gy") == 0
    full = jnp.where(first, jnp.stack([column, partner], axis=1), jnp.stack([partner, column], axis=1))
    return full.reshape(1, 2 * nz, *piece.shape)


def per_device_body(source_field, clover, forward, backward, restrict_blocks):
    first_image = operate(source_field, clover, forward, backward)
    second_image = operate(first_image, clover, forward, backward)
    partial_sum = jnp.einsum(
        "tzyxij,tzyxrj->ri", restrict_blocks, second_image, preferred_element_type=jnp.float32
    )
    restricted = gather_pieces(partial_sum.astype(jnp.bfloat16))
    return (second_image, restricted)


def solution(mesh):
    return jax.shard_map(
        per_device_body,
        mesh=mesh,
        in_specs=(
            P("ta", "gz", "gy", None, None, None),
            P("ta", "gz", "gy", None, None, None),
            P(None, "ta", "gz", "gy", None, None, None),
            P(None, "ta", "gz", "gy", None, None, None),
            P("ta", "gz", "gy", None, None, None),
        ),
        out_specs=(P("ta", "gz", "gy", None, None, None), P("ta", None, None, None)),
        check_vma=False,
    )
```

```python
import jax
import jax.numpy as jnp
from jax import lax
from jax.sharding import PartitionSpec as P


def apply_block(blocks, vector):
    return jnp.einsum("tzyxij,tzyxrj->tzyxri", blocks, vector, preferred_element_type=jnp.float32)


def formed(blocks, vector):
    return lax.optimization_barrier(apply_block(blocks, vector).astype(jnp.bfloat16))


def ring(n, step):
    return [(i, (i + step) % n) for i in range(n)]


def take(block, dim, start, stop):
    return lax.slice_in_dim(block, start, stop, axis=dim)


def neighbours(vector, pulled, dim, axis):
    count = lax.axis_size(axis)
    size = vector.shape[dim]
    first = take(vector, dim, 0, 1)
    last = take(pulled, dim, size - 1, size)
    if count == 2:
        both = lax.ppermute(jnp.stack([first, last]), axis, ring(2, 1))
        got_v, got_p = both[0], both[1]
    else:
        got_v = lax.ppermute(first, axis, ring(count, -1))
        got_p = lax.ppermute(last, axis, ring(count, 1))
    ahead = jnp.concatenate([take(vector, dim, 1, size), got_v], axis=dim)
    behind = jnp.concatenate([got_p, take(pulled, dim, 0, size - 1)], axis=dim)
    return ahead, behind


AXES = ((0, "ta"), (1, "gz"), (2, "gy"))


def operate(vector, clover, forward, backward):
    pulled = [formed(backward[m], vector) for m in range(4)]
    terms = []
    pulls = []
    for m, axis in AXES:
        ahead, behind = neighbours(vector, pulled[m], m, axis)
        terms.append(apply_block(forward[m], ahead))
        pulls.append(behind)
    terms.append(apply_block(forward[3], jnp.roll(vector, -1, axis=3)))
    pulls.append(jnp.roll(pulled[3], 1, axis=3))
    total = apply_block(clover, vector)
    for term in terms:
        total = total + term
    for pull in pulls:
        total = total + pull.astype(jnp.float32)
    return total.astype(jnp.bfloat16)


def gather_pieces(piece):
    nz = lax.axis_size("gz")
    assert lax.axis_size("gy") == 2
    copies = jnp.broadcast_to(piece[None], (nz, *piece.shape))
    column = lax.all_to_all(copies, "gz", 0, 0, tiled=True)
    partner = lax.ppermute(column, "gy", ring(2, 1))
    first = lax.axis_index("gy") == 0
    full = jnp.where(first, jnp.stack([column, partner], axis=1), jnp.stack([partner, column], axis=1))
    return full.reshape(1, 2 * nz, *piece.shape)


HALVES = 2


def per_device_body(source_field, clover, forward, backward, restrict_blocks):
    first_image = operate(source_field, clover, forward, backward)
    rows = first_image.shape[4] // HALVES
    images, pieces = [], []
    for h in range(HALVES):
        part = lax.slice_in_dim(first_image, h * rows, (h + 1) * rows, axis=4)
        image = operate(part, clover, forward, backward)
        partial_sum = jnp.einsum(
            "tzyxij,tzyxrj->ri", restrict_blocks, image, preferred_element_type=jnp.float32
        )
        pieces.append(gather_pieces(partial_sum.astype(jnp.bfloat16)))
        images.append(image)
    return jnp.concatenate(images, axis=4), jnp.concatenate(pieces, axis=2)


def solution(mesh):
    return jax.shard_map(
        per_device_body,
        mesh=mesh,
        in_specs=(
            P("ta", "gz", "gy", None, None, None),
            P("ta", "gz", "gy", None, None, None),
            P(None, "ta", "gz", "gy", None, None, None),
            P(None, "ta", "gz", "gy", None, None, None),
            P("ta", "gz", "gy", None, None, None),
        ),
        out_specs=(P("ta", "gz", "gy", None, None, None), P("ta", None, None, None)),
        check_vma=False,
    )
```

```python
import jax
import jax.numpy as jnp
from jax import lax
from jax.sharding import PartitionSpec as P


def apply_block(blocks, vector):
    return jnp.einsum("tzyxij,tzyxrj->tzyxri", blocks, vector, preferred_element_type=jnp.float32)


def formed(blocks, vector):
    return lax.optimization_barrier(apply_block(blocks, vector).astype(jnp.bfloat16))


def ring(n, step):
    return [(i, (i + step) % n) for i in range(n)]


def take(block, dim, start, stop):
    return lax.slice_in_dim(block, start, stop, axis=dim)


def neighbours(vector, pulled, dim, axis):
    count = lax.axis_size(axis)
    size = vector.shape[dim]
    first = take(vector, dim, 0, 1)
    last = take(pulled, dim, size - 1, size)
    if count == 2:
        both = lax.ppermute(jnp.stack([first, last]), axis, ring(2, 1))
        got_v, got_p = both[0], both[1]
    else:
        got_v = lax.ppermute(first, axis, ring(count, -1))
        got_p = lax.ppermute(last, axis, ring(count, 1))
    ahead = jnp.concatenate([take(vector, dim, 1, size), got_v], axis=dim)
    behind = jnp.concatenate([got_p, take(pulled, dim, 0, size - 1)], axis=dim)
    return ahead, behind


AXES = ((0, "ta"), (1, "gz"), (2, "gy"))


def operate(vector, clover, forward, backward):
    pulled = [formed(backward[m], vector) for m in range(4)]
    terms = []
    pulls = []
    for m, axis in AXES:
        ahead, behind = neighbours(vector, pulled[m], m, axis)
        terms.append(apply_block(forward[m], ahead))
        pulls.append(behind)
    terms.append(apply_block(forward[3], jnp.roll(vector, -1, axis=3)))
    pulls.append(jnp.roll(pulled[3], 1, axis=3))
    total = apply_block(clover, vector)
    for term in terms:
        total = total + term
    for pull in pulls:
        total = total + pull.astype(jnp.float32)
    return total.astype(jnp.bfloat16)


def gather_pieces(piece):
    nz = lax.axis_size("gz")
    assert lax.axis_size("gy") == 2
    copies = jnp.broadcast_to(piece[None], (nz, *piece.shape))
    column = lax.all_to_all(copies, "gz", 0, 0, tiled=True)
    both = jnp.broadcast_to(column[:, None], (nz, 2, *piece.shape))
    full = lax.all_to_all(both, "gy", 1, 1, tiled=True)
    return full.reshape(1, 2 * nz, *piece.shape)


def per_device_body(source_field, clover, forward, backward, restrict_blocks):
    first_image = operate(source_field, clover, forward, backward)
    second_image = operate(first_image, clover, forward, backward)
    partial_sum = jnp.einsum(
        "tzyxij,tzyxrj->ri", restrict_blocks, second_image, preferred_element_type=jnp.float32
    )
    restricted = gather_pieces(partial_sum.astype(jnp.bfloat16))
    return (second_image, restricted)


def solution(mesh):
    return jax.shard_map(
        per_device_body,
        mesh=mesh,
        in_specs=(
            P("ta", "gz", "gy", None, None, None),
            P("ta", "gz", "gy", None, None, None),
            P(None, "ta", "gz", "gy", None, None, None),
            P(None, "ta", "gz", "gy", None, None, None),
            P("ta", "gz", "gy", None, None, None),
        ),
        out_specs=(P("ta", "gz", "gy", None, None, None), P("ta", None, None, None)),
        check_vma=False,
    )
```
